1024 devices in a mesh: seq: 16 (over z_lo, core), head: 64 (over z_hi, x, y).
Axes of the slice: x: 4, y: 8, z: 16 (z_hi: 2, z_lo: 8; z = z_hi * 8 + z_lo), core: 2. Of those that a mesh axis runs over, the one named last changes fastest.
Arguments:
- queries: float32 [4096, 4096], P('seq', 'head'), may hold values from -50 to 50
- keys: float32 [4096, 4096], P('seq', 'head'), may hold values from -16 to 16
- values: float32 [4096, 4096], P('seq', 'head'), may hold values from -6 to 6
- local_span: int32 [32], replicated, may hold values from 1 to 2
- wo_local: float32 [4096, 4096], P('head'), may hold values from -0.1875 to 0.1875
- wo_strided: float32 [4096, 4096], P('head'), may hold values from -0.1875 to 0.1875
- grad_out: bfloat16 [4096, 4096], P('seq', 'head'), may hold values from -6 to 6
Outputs:
- mixed: float32 [4096, 4096], P('seq', 'head')
- grad_queries: float32 [4096, 4096], P('seq', 'head')
- grad_keys: float32 [4096, 4096], P('seq', 'head')
- grad_values: float32 [4096, 4096], P('seq', 'head')
The draws below stay inside these ranges and needn't reach their ends.
All inputs are finite; a program needn't handle non-finite values.
Results may differ from the reference program's by a relative error of at most 0.0003.
Values may be sent and summed in bfloat16 or wider, within the bound.
No kernel may reach another device: no remote copies, remote signals or barrier semaphores. Data moves between devices by JAX's collectives and lax.ppermute only.
A program may use at most 32 MiB of HBM per device.

```python
import jax
import jax.numpy as jnp
from jax import lax

D = 4096
HDIM = 128
BLOCK = 128
GROUP_BLK = 2
STRIDE = 128
TOKENS = 4096
HEADS = 32


def query_key_pair(key):
    base = jax.random.fold_in(key, 7)
    key_q, key_k = jax.random.split(base, 2)
    layout = (TOKENS, HEADS, HDIM)
    query_all = jnp.clip(jax.random.normal(key_q, layout, jnp.float32), -6.0, 6.0)
    key_all = jnp.clip(jax.random.normal(key_k, layout, jnp.float32), -6.0, 6.0)
    return (query_all.reshape(TOKENS, HEADS * HDIM), key_all.reshape(TOKENS, HEADS * HDIM))


def draw_queries(key, part):
    return query_key_pair(key)[0]


def draw_keys(key, part):
    return query_key_pair(key)[1]


def draw_local_span(key, part):
    key_one, key_two = jax.random.split(jax.random.fold_in(key, 11))
    spans = jax.random.randint(key_one, (HEADS,), 1, GROUP_BLK + 1)
    picked = jax.random.randint(key_two, (), 0, HEADS)
    return jnp.where(jnp.arange(HEADS) == picked, GROUP_BLK, spans).astype(jnp.int32)


def spiked(drawn, own_key, source, target, parts, factor):
    owner, partner = [(jnp.arange(drawn.shape[axis_at]) // (drawn.shape[axis_at] // parts)).reshape([-1 if axis == axis_at else 1 for axis in range(drawn.ndim)]) for axis_at in (source, target)]
    chosen = jax.random.permutation(own_key, parts)[partner]
    strong = (owner == chosen) | (owner == (partner + parts // 2) % parts)
    return jnp.where(strong, factor * drawn, drawn)


def shard_levels(key, dims, shards, smallest, high):
    def one(dim, parts):
        heights = jax.random.uniform(jax.random.fold_in(jax.random.fold_in(key, 6), dim), (parts,), jnp.float32, smallest / len(shards), high / len(shards))
        return jnp.repeat(jnp.exp(heights), dims[dim] // parts).reshape((-1,) + (1,) * (len(dims) - dim - 1))

    factor_of = one(*shards[0])
    for cut in shards[1:]:
        factor_of = factor_of * one(*cut)
    return factor_of


def noise(rng, shape, deviation, most, cuts=(), held_as=jnp.bfloat16):
    level = shard_levels(rng, shape, cuts, -0.22, 0.18) if cuts else 1.0
    result = jax.random.normal(rng, shape, jnp.float32) * deviation * level
    return jnp.minimum(jnp.maximum(result, -most), most).astype(held_as)


def bell_draw_with(rng, shape, spread, limit, cuts, heavy, held_as=jnp.bfloat16):
    entries = spread * jax.random.normal(rng, shape, jnp.float32)
    if cuts:
        entries = entries * shard_levels(rng, shape, cuts, -0.22, 0.18)
    return jnp.clip(spiked(entries, jax.random.fold_in(rng, 3), *heavy), -limit, limit).astype(held_as)


def setup_inputs(seed: int = 0) -> dict:
    arg_keys = jax.random.split(jax.random.key(seed), 8)
    queries = draw_queries(jax.random.fold_in(arg_keys[7], 71), 0)
    keys = draw_keys(jax.random.fold_in(arg_keys[7], 71), 0)
    values = noise(arg_keys[2], (TOKENS, HEADS * HDIM), 1.0, 6.0, ((0, 16), (1, 64)), jnp.float32)
    local_span = draw_local_span(jax.random.fold_in(arg_keys[7], 71), 0)
    wo_local = bell_draw_with(arg_keys[4], (HEADS * HDIM, D), (2 * HEADS * HDIM) ** -0.5, 0.1875, ((0, 64),), (0, 1, 64, 4.0), jnp.float32)
    wo_strided = bell_draw_with(arg_keys[5], (HEADS * HDIM, D), (2 * HEADS * HDIM) ** -0.5, 0.1875, ((0, 64),), (0, 1, 64, 4.0), jnp.float32)
    grad_out = noise(arg_keys[6], (TOKENS, D), 1.0, 6.0, ((0, 16), (1, 64)))
    return {"queries": queries, "keys": keys, "values": values, "local_span": local_span, "wo_local": wo_local, "wo_strided": wo_strided, "grad_out": grad_out}


HIGHEST = lax.Precision.HIGHEST


def attend_forward(query_part, key_part, value_part, allowed):
    scale_factor = HDIM ** -0.5
    scores = jnp.einsum("bqhd,bkhd->bhqk", query_part, key_part, precision=HIGHEST) * scale_factor
    row_max = jnp.max(jnp.where(allowed, scores, -jnp.inf), axis=-1, keepdims=True)
    weights = jnp.where(allowed, jnp.exp(scores - row_max), 0.0)
    probs = weights / jnp.sum(weights, axis=-1, keepdims=True)
    attended = jnp.einsum("bhqk,bkhd->bqhd", probs, value_part, precision=HIGHEST)
    return attended, probs


def attend_backward(query_part, key_part, value_part, probs, attended, incoming):
    scale_factor = HDIM ** -0.5
    dprobs = jnp.einsum("bqhd,bkhd->bhqk", incoming, value_part, precision=HIGHEST)
    row_delta = jnp.transpose(jnp.sum(incoming * attended, axis=-1), (0, 2, 1))[..., None]
    dscores = probs * (dprobs - row_delta)
    grad_query = jnp.einsum("bhqk,bkhd->bqhd", dscores, key_part, precision=HIGHEST) * scale_factor
    grad_key = jnp.einsum("bhqk,bqhd->bkhd", dscores, query_part, precision=HIGHEST) * scale_factor
    grad_value = jnp.einsum("bhqk,bqhd->bkhd", probs, incoming, precision=HIGHEST)
    return grad_query, grad_key, grad_value


def reference(queries, keys, values, local_span, wo_local, wo_strided, grad_out):
    group_len = GROUP_BLK * BLOCK
    groups = TOKENS // group_len
    runs = TOKENS // STRIDE
    local_layout = (groups, group_len, HEADS, HDIM)
    local_q = queries.reshape(local_layout)
    local_k = keys.reshape(local_layout)
    local_v = values.reshape(local_layout)
    position = jnp.arange(group_len)
    block_of = position // BLOCK
    causal = position[None, None, :] <= position[None, :, None]
    reach = (block_of[None, :, None] - block_of[None, None, :]) < local_span[:, None, None]
    allowed_local = (causal & reach)[None]

    def to_runs(matrix):
        return matrix.reshape(runs, STRIDE, HEADS, HDIM).transpose(1, 0, 2, 3)

    def from_runs(stacked):
        return stacked.transpose(1, 0, 2, 3).reshape(TOKENS, HEADS * HDIM)

    strided_q = to_runs(queries)
    strided_k = to_runs(keys)
    strided_v = to_runs(values)
    order = jnp.arange(runs)
    allowed_strided = (order[None, :] <= order[:, None])[None, None]

    attn_local, probs_local = attend_forward(local_q, local_k, local_v, allowed_local)
    attn_strided, probs_strided = attend_forward(strided_q, strided_k, strided_v, allowed_strided)
    flat_local = attn_local.reshape(TOKENS, HEADS * HDIM)
    flat_strided = from_runs(attn_strided)
    mixed = jnp.dot(flat_local, wo_local, precision=HIGHEST, preferred_element_type=jnp.float32)
    mixed = mixed + jnp.dot(flat_strided, wo_strided, precision=HIGHEST, preferred_element_type=jnp.float32)

    grad_all = grad_out.astype(jnp.float32)
    grad_local = jnp.dot(grad_all, wo_local.T, precision=HIGHEST, preferred_element_type=jnp.float32)
    grad_strided = jnp.dot(grad_all, wo_strided.T, precision=HIGHEST, preferred_element_type=jnp.float32)
    dq_local, dk_local, dv_local = attend_backward(local_q, local_k, local_v, probs_local, attn_local, grad_local.reshape(local_layout))
    dq_strided, dk_strided, dv_strided = attend_backward(strided_q, strided_k, strided_v, probs_strided, attn_strided, to_runs(grad_strided))
    grad_queries = dq_local.reshape(TOKENS, HEADS * HDIM) + from_runs(dq_strided)
    grad_keys = dk_local.reshape(TOKENS, HEADS * HDIM) + from_runs(dk_strided)
    grad_values = dv_local.reshape(TOKENS, HEADS * HDIM) + from_runs(dv_strided)
    return (mixed, grad_queries, grad_keys, grad_values)
```

```python
import jax
import jax.numpy as jnp
from jax import lax
from jax.sharding import PartitionSpec as P

HDIM = 128
BLOCK = 128
GROUP_BLK = 2
STRIDE = 128


HIGHEST = lax.Precision.HIGHEST


HEAD_AXES = ("zh", "x", "y")


def swapped(x, axis, distance):
    return lax.ppermute(x, axis, [(i, i ^ 1 << distance) for i in range(lax.axis_size(axis))])


def pair_sum(partial_value):
    return partial_value + swapped(partial_value, "y", 0)


def head_index():
    return (lax.axis_index("zh") * lax.axis_size("x") + lax.axis_index("x")) * lax.axis_size("y") + lax.axis_index("y")


def scatter_head(partial_value):
    sizes = [lax.axis_size(a) for a in HEAD_AXES]
    rows, cols = partial_value.shape
    block = rows // (sizes[0] * sizes[1] * sizes[2])
    parts = partial_value.reshape(*sizes, block, cols)
    for dim in (2, 1, 0):
        parts = lax.all_to_all(parts, HEAD_AXES[dim], dim, dim, tiled=True).sum(dim)
    return parts


def gather_head(piece):
    return lax.all_gather(piece, HEAD_AXES, axis=1, tiled=True)


def attend_forward(query_part, key_part, value_part, allowed):
    scale_factor = HDIM ** (-0.5)
    partial_value = jnp.einsum("bqhd,bkhd->bhqk", query_part, key_part, precision=HIGHEST)
    scores = pair_sum(partial_value) * scale_factor
    row_max = jnp.max(jnp.where(allowed, scores, -jnp.inf), axis=-1, keepdims=True)
    weights = jnp.where(allowed, jnp.exp(scores - row_max), 0.0)
    probs = weights / jnp.sum(weights, axis=-1, keepdims=True)
    attended = jnp.einsum("bhqk,bkhd->bqhd", probs, value_part, precision=HIGHEST)
    return (attended, probs)


def attend_backward(query_part, key_part, value_part, probs, attended, incoming):
    scale_factor = HDIM ** (-0.5)
    dprobs_part = jnp.einsum("bqhd,bkhd->bhqk", incoming, value_part, precision=HIGHEST)
    delta_part = jnp.transpose(jnp.sum(incoming * attended, axis=-1), (0, 2, 1))[..., None]
    joined = pair_sum(jnp.concatenate([dprobs_part, delta_part], axis=-1))
    dprobs = joined[..., :-1]
    row_delta = joined[..., -1:]
    dscores = probs * (dprobs - row_delta)
    grad_query = jnp.einsum("bhqk,bkhd->bqhd", dscores, key_part, precision=HIGHEST) * scale_factor
    grad_key = jnp.einsum("bhqk,bqhd->bkhd", dscores, query_part, precision=HIGHEST) * scale_factor
    grad_value = jnp.einsum("bhqk,bqhd->bkhd", probs, incoming, precision=HIGHEST)
    return (grad_query, grad_key, grad_value)


def to_strided(stacked):
    seq_devices = lax.axis_size("seq")
    tok_rows, members, head_dim = stacked.shape
    layout = stacked.reshape(tok_rows // seq_devices, seq_devices, members, head_dim)
    moved = lax.all_to_all(layout, "seq", split_axis=1, concat_axis=0, tiled=True)
    return moved.reshape(tok_rows, members, head_dim)


def to_contiguous(stacked):
    seq_devices = lax.axis_size("seq")
    tok_rows, members, head_dim = stacked.shape
    layout = stacked.reshape(seq_devices, tok_rows // seq_devices, 1, members, head_dim)
    moved = lax.all_to_all(layout, "seq", split_axis=0, concat_axis=2, tiled=True)
    return moved.reshape(tok_rows, members, head_dim)


def local(queries, keys, values, local_span, wo_local, wo_strided, grad_out):
    tok_rows, head_dim = queries.shape
    seq_devices = lax.axis_size("seq")
    per_run = STRIDE // seq_devices
    runs_here = tok_rows // per_run
    group_len = GROUP_BLK * BLOCK
    local_layout = (tok_rows // group_len, group_len, 1, head_dim)
    own_span = local_span[head_index() // 2]
    stacked = jnp.stack([queries, keys, values], axis=1)
    spread = to_strided(stacked)
    local_q = queries.reshape(local_layout)
    local_k = keys.reshape(local_layout)
    local_v = values.reshape(local_layout)
    position = jnp.arange(group_len)
    block_of = position // BLOCK
    causal = position[None, :] <= position[:, None]
    reach = block_of[:, None] - block_of[None, :] < own_span
    allowed_local = (causal & reach)[None, None]
    attn_local, probs_local = attend_forward(local_q, local_k, local_v, allowed_local)

    def to_runs(matrix):
        return matrix.reshape(runs_here, per_run, 1, head_dim).transpose(1, 0, 2, 3)

    def from_runs(arranged):
        return arranged.transpose(1, 0, 2, 3).reshape(tok_rows, head_dim)

    strided_q = to_runs(spread[:, 0])
    strided_k = to_runs(spread[:, 1])
    strided_v = to_runs(spread[:, 2])
    order = jnp.arange(runs_here)
    allowed_strided = (order[None, :] <= order[:, None])[None, None]
    attn_strided, probs_strided = attend_forward(strided_q, strided_k, strided_v, allowed_strided)
    strided_home = to_contiguous(from_runs(attn_strided)[:, None, :])[:, 0]
    attn_both = jnp.concatenate([attn_local.reshape(tok_rows, head_dim), strided_home], axis=1)
    wo_both = jnp.concatenate([wo_local, wo_strided], axis=0)
    w_cols = wo_both
    mixed_cols = scatter_head(
        lax.dot_general(
            w_cols,
            attn_both,
            (((0,), (1,)), ((), ())),
            precision=HIGHEST,
            preferred_element_type=jnp.float32,
        )
    )
    mixed = mixed_cols.T
    w_cols = wo_both
    grad_both = lax.dot_general(
        gather_head(grad_out).astype(jnp.float32),
        w_cols,
        (((1,), (1,)), ((), ())),
        precision=HIGHEST,
        preferred_element_type=jnp.float32,
    )
    grad_local = grad_both[:, :head_dim]
    grad_strided = to_strided(grad_both[:, head_dim:][:, None, :])[:, 0]
    dq_local, dk_local, dv_local = attend_backward(
        local_q, local_k, local_v, probs_local, attn_local, grad_local.reshape(local_layout)
    )
    dq_strided, dk_strided, dv_strided = attend_backward(
        strided_q, strided_k, strided_v, probs_strided, attn_strided, to_runs(grad_strided)
    )
    strided_grads = jnp.stack(
        [from_runs(dq_strided), from_runs(dk_strided), from_runs(dv_strided)], axis=1
    )
    grads_home = to_contiguous(strided_grads)
    grad_queries = dq_local.reshape(tok_rows, head_dim) + grads_home[:, 0]
    grad_keys = dk_local.reshape(tok_rows, head_dim) + grads_home[:, 1]
    grad_values = dv_local.reshape(tok_rows, head_dim) + grads_home[:, 2]
    return (mixed, grad_queries, grad_keys, grad_values)


def solution(mesh):
    seq_size, head_size = mesh.devices.shape
    zh = 2
    xs = 4
    view = jax.sharding.Mesh(mesh.devices.reshape(seq_size, zh, xs, head_size // (zh * xs)), ("seq",) + HEAD_AXES)
    return jax.shard_map(
        local,
        mesh=view,
        in_specs=(
            P("seq", HEAD_AXES),
            P("seq", HEAD_AXES),
            P("seq", HEAD_AXES),
            P(),
            P(HEAD_AXES, None),
            P(HEAD_AXES, None),
            P("seq", HEAD_AXES),
        ),
        out_specs=(P("seq", HEAD_AXES), P("seq", HEAD_AXES), P("seq", HEAD_AXES), P("seq", HEAD_AXES)),
        check_vma=False,
    )
```

```python
import jax
import jax.numpy as jnp
from jax import lax
from jax.sharding import PartitionSpec as P

HDIM = 128
BLOCK = 128
GROUP_BLK = 2
STRIDE = 128


HIGHEST = lax.Precision.HIGHEST


HEAD_AXES = ("zh", "x", "y")


def swapped(x, axis, distance):
    return lax.ppermute(x, axis, [(i, i ^ 1 << distance) for i in range(lax.axis_size(axis))])


def pair_sum(partial_value):
    return partial_value + swapped(partial_value, "y", 0)


def head_index():
    return (lax.axis_index("zh") * lax.axis_size("x") + lax.axis_index("x")) * lax.axis_size("y") + lax.axis_index("y")


def scatter_head(partial_value, companion):
    sizes = [lax.axis_size(a) for a in HEAD_AXES]
    rows, cols = partial_value.shape
    block = rows // (sizes[0] * sizes[1] * sizes[2])
    parts = partial_value.reshape(*sizes, block, cols)
    for dim in (2, 1, 0):
        parts = lax.all_to_all(parts, HEAD_AXES[dim], dim, dim, tiled=True).sum(dim)
        if dim == 2:
            parts, companion = lax.optimization_barrier((parts, companion))
    return parts, companion


def gather_head(piece):
    return lax.all_gather(piece, HEAD_AXES, axis=1, tiled=True)


def attend_forward(query_part, key_part, value_part, allowed):
    scale_factor = HDIM ** (-0.5)
    partial_value = jnp.einsum("bqhd,bkhd->bhqk", query_part, key_part, precision=HIGHEST)
    scores = pair_sum(partial_value) * scale_factor
    row_max = jnp.max(jnp.where(allowed, scores, -jnp.inf), axis=-1, keepdims=True)
    weights = jnp.where(allowed, jnp.exp(scores - row_max), 0.0)
    probs = weights / jnp.sum(weights, axis=-1, keepdims=True)
    attended = jnp.einsum("bhqk,bkhd->bqhd", probs, value_part, precision=HIGHEST)
    return (attended, probs)


def attend_backward(query_part, key_part, value_part, probs, attended, incoming):
    scale_factor = HDIM ** (-0.5)
    dprobs_part = jnp.einsum("bqhd,bkhd->bhqk", incoming, value_part, precision=HIGHEST)
    delta_part = jnp.transpose(jnp.sum(incoming * attended, axis=-1), (0, 2, 1))[..., None]
    joined = pair_sum(jnp.concatenate([dprobs_part, delta_part], axis=-1))
    dprobs = joined[..., :-1]
    row_delta = joined[..., -1:]
    dscores = probs * (dprobs - row_delta)
    grad_query = jnp.einsum("bhqk,bkhd->bqhd", dscores, key_part, precision=HIGHEST) * scale_factor
    grad_key = jnp.einsum("bhqk,bqhd->bkhd", dscores, query_part, precision=HIGHEST) * scale_factor
    grad_value = jnp.einsum("bhqk,bqhd->bkhd", probs, incoming, precision=HIGHEST)
    return (grad_query, grad_key, grad_value)


def to_strided(stacked):
    seq_devices = lax.axis_size("seq")
    tok_rows, members, head_dim = stacked.shape
    layout = stacked.reshape(tok_rows // seq_devices, seq_devices, members, head_dim)
    moved = lax.all_to_all(layout, "seq", split_axis=1, concat_axis=0, tiled=True)
    return moved.reshape(tok_rows, members, head_dim)


def to_contiguous(stacked):
    seq_devices = lax.axis_size("seq")
    tok_rows, members, head_dim = stacked.shape
    layout = stacked.reshape(seq_devices, tok_rows // seq_devices, 1, members, head_dim)
    moved = lax.all_to_all(layout, "seq", split_axis=0, concat_axis=2, tiled=True)
    return moved.reshape(tok_rows, members, head_dim)


def local(queries, keys, values, local_span, wo_local, wo_strided, grad_out):
    tok_rows, head_dim = queries.shape
    seq_devices = lax.axis_size("seq")
    per_run = STRIDE // seq_devices
    runs_here = tok_rows // per_run
    group_len = GROUP_BLK * BLOCK
    local_layout = (tok_rows // group_len, group_len, 1, head_dim)
    own_span = local_span[head_index() // 2]
    stacked = jnp.stack([queries, keys, values], axis=1)
    spread = to_strided(stacked)
    local_q = queries.reshape(local_layout)
    local_k = keys.reshape(local_layout)
    local_v = values.reshape(local_layout)
    position = jnp.arange(group_len)
    block_of = position // BLOCK
    causal = position[None, :] <= position[:, None]
    reach = block_of[:, None] - block_of[None, :] < own_span
    allowed_local = (causal & reach)[None, None]
    attn_local, probs_local = attend_forward(local_q, local_k, local_v, allowed_local)

    def to_runs(matrix):
        return matrix.reshape(runs_here, per_run, 1, head_dim).transpose(1, 0, 2, 3)

    def from_runs(arranged):
        return arranged.transpose(1, 0, 2, 3).reshape(tok_rows, head_dim)

    strided_q = to_runs(spread[:, 0])
    strided_k = to_runs(spread[:, 1])
    strided_v = to_runs(spread[:, 2])
    order = jnp.arange(runs_here)
    allowed_strided = (order[None, :] <= order[:, None])[None, None]
    attn_strided, probs_strided = attend_forward(strided_q, strided_k, strided_v, allowed_strided)
    strided_home = to_contiguous(from_runs(attn_strided)[:, None, :])[:, 0]
    attn_both = jnp.concatenate([attn_local.reshape(tok_rows, head_dim), strided_home], axis=1)
    wo_both = jnp.concatenate([wo_local, wo_strided], axis=0)
    w_cols = wo_both
    mixed_cols, grad_rows = scatter_head(
        lax.dot_general(
            w_cols,
            attn_both,
            (((0,), (1,)), ((), ())),
            precision=HIGHEST,
            preferred_element_type=jnp.float32,
        ),
        gather_head(grad_out),
    )
    mixed = mixed_cols.T
    w_cols = wo_both
    grad_both = lax.dot_general(
        grad_rows.astype(jnp.float32),
        w_cols,
        (((1,), (1,)), ((), ())),
        precision=HIGHEST,
        preferred_element_type=jnp.float32,
    )
    grad_local = grad_both[:, :head_dim]
    grad_strided = to_strided(grad_both[:, head_dim:][:, None, :])[:, 0]
    dq_local, dk_local, dv_local = attend_backward(
        local_q, local_k, local_v, probs_local, attn_local, grad_local.reshape(local_layout)
    )
    dq_strided, dk_strided, dv_strided = attend_backward(
        strided_q, strided_k, strided_v, probs_strided, attn_strided, to_runs(grad_strided)
    )
    strided_grads = jnp.stack(
        [from_runs(dq_strided), from_runs(dk_strided), from_runs(dv_strided)], axis=1
    )
    grads_home = to_contiguous(strided_grads)
    grad_queries = dq_local.reshape(tok_rows, head_dim) + grads_home[:, 0]
    grad_keys = dk_local.reshape(tok_rows, head_dim) + grads_home[:, 1]
    grad_values = dv_local.reshape(tok_rows, head_dim) + grads_home[:, 2]
    return (mixed, grad_queries, grad_keys, grad_values)


def solution(mesh):
    seq_size, head_size = mesh.devices.shape
    zh = 2
    xs = 4
    view = jax.sharding.Mesh(mesh.devices.reshape(seq_size, zh, xs, head_size // (zh * xs)), ("seq",) + HEAD_AXES)
    return jax.shard_map(
        local,
        mesh=view,
        in_specs=(
            P("seq", HEAD_AXES),
            P("seq", HEAD_AXES),
            P("seq", HEAD_AXES),
            P(),
            P(HEAD_AXES, None),
            P(HEAD_AXES, None),
            P("seq", HEAD_AXES),
        ),
        out_specs=(P("seq", HEAD_AXES), P("seq", HEAD_AXES), P("seq", HEAD_AXES), P("seq", HEAD_AXES)),
        check_vma=False,
    )
```

```python
import jax
import jax.numpy as jnp
from jax import lax
from jax.sharding import PartitionSpec as P

HDIM = 128
BLOCK = 128
GROUP_BLK = 2
STRIDE = 128


HIGHEST = lax.Precision.HIGHEST


HEAD_AXES = ("zh", "x", "y")


def swapped(x, axis, distance):
    return lax.ppermute(x, axis, [(i, i ^ 1 << distance) for i in range(lax.axis_size(axis))])


def pair_sum(partial_value):
    return partial_value + swapped(partial_value, "y", 0)


def head_index():
    return (lax.axis_index("zh") * lax.axis_size("x") + lax.axis_index("x")) * lax.axis_size("y") + lax.axis_index("y")


def scatter_head(partial_value, companion):
    sizes = [lax.axis_size(a) for a in HEAD_AXES]
    rows, cols = partial_value.shape
    block = rows // (sizes[0] * sizes[1] * sizes[2])
    parts = partial_value.reshape(*sizes, block, cols)
    parts = lax.all_to_all(parts, "x", 1, 1, tiled=True).sum(1)
    parts, companion = lax.optimization_barrier((parts, companion))
    for dim in (1, 0):
        parts = lax.all_to_all(parts, HEAD_AXES[2 * dim], dim, dim, tiled=True).sum(dim)
    return parts, companion


def gather_head(piece):
    return lax.all_gather(piece, HEAD_AXES, axis=1, tiled=True)


def attend_forward(query_part, key_part, value_part, allowed):
    scale_factor = HDIM ** (-0.5)
    partial_value = jnp.einsum("bqhd,bkhd->bhqk", query_part, key_part, precision=HIGHEST)
    scores = pair_sum(partial_value) * scale_factor
    row_max = jnp.max(jnp.where(allowed, scores, -jnp.inf), axis=-1, keepdims=True)
    weights = jnp.where(allowed, jnp.exp(scores - row_max), 0.0)
    probs = weights / jnp.sum(weights, axis=-1, keepdims=True)
    attended = jnp.einsum("bhqk,bkhd->bqhd", probs, value_part, precision=HIGHEST)
    return (attended, probs)


def attend_backward(query_part, key_part, value_part, probs, attended, incoming):
    scale_factor = HDIM ** (-0.5)
    dprobs_part = jnp.einsum("bqhd,bkhd->bhqk", incoming, value_part, precision=HIGHEST)
    delta_part = jnp.transpose(jnp.sum(incoming * attended, axis=-1), (0, 2, 1))[..., None]
    joined = pair_sum(jnp.concatenate([dprobs_part, delta_part], axis=-1))
    dprobs = joined[..., :-1]
    row_delta = joined[..., -1:]
    dscores = probs * (dprobs - row_delta)
    grad_query = jnp.einsum("bhqk,bkhd->bqhd", dscores, key_part, precision=HIGHEST) * scale_factor
    grad_key = jnp.einsum("bhqk,bqhd->bkhd", dscores, query_part, precision=HIGHEST) * scale_factor
    grad_value = jnp.einsum("bhqk,bqhd->bkhd", probs, incoming, precision=HIGHEST)
    return (grad_query, grad_key, grad_value)


def to_strided(stacked):
    seq_devices = lax.axis_size("seq")
    tok_rows, members, head_dim = stacked.shape
    layout = stacked.reshape(tok_rows // seq_devices, seq_devices, members, head_dim)
    moved = lax.all_to_all(layout, "seq", split_axis=1, concat_axis=0, tiled=True)
    return moved.reshape(tok_rows, members, head_dim)


def to_contiguous(stacked):
    seq_devices = lax.axis_size("seq")
    tok_rows, members, head_dim = stacked.shape
    layout = stacked.reshape(seq_devices, tok_rows // seq_devices, 1, members, head_dim)
    moved = lax.all_to_all(layout, "seq", split_axis=0, concat_axis=2, tiled=True)
    return moved.reshape(tok_rows, members, head_dim)


def local(queries, keys, values, local_span, wo_local, wo_strided, grad_out):
    tok_rows, head_dim = queries.shape
    seq_devices = lax.axis_size("seq")
    per_run = STRIDE // seq_devices
    runs_here = tok_rows // per_run
    group_len = GROUP_BLK * BLOCK
    local_layout = (tok_rows // group_len, group_len, 1, head_dim)
    own_span = local_span[head_index() // 2]
    stacked = jnp.stack([queries, keys, values], axis=1)
    spread = to_strided(stacked)
    local_q = queries.reshape(local_layout)
    local_k = keys.reshape(local_layout)
    local_v = values.reshape(local_layout)
    position = jnp.arange(group_len)
    block_of = position // BLOCK
    causal = position[None, :] <= position[:, None]
    reach = block_of[:, None] - block_of[None, :] < own_span
    allowed_local = (causal & reach)[None, None]
    attn_local, probs_local = attend_forward(local_q, local_k, local_v, allowed_local)

    def to_runs(matrix):
        return matrix.reshape(runs_here, per_run, 1, head_dim).transpose(1, 0, 2, 3)

    def from_runs(arranged):
        return arranged.transpose(1, 0, 2, 3).reshape(tok_rows, head_dim)

    strided_q = to_runs(spread[:, 0])
    strided_k = to_runs(spread[:, 1])
    strided_v = to_runs(spread[:, 2])
    order = jnp.arange(runs_here)
    allowed_strided = (order[None, :] <= order[:, None])[None, None]
    attn_strided, probs_strided = attend_forward(strided_q, strided_k, strided_v, allowed_strided)
    strided_home = to_contiguous(from_runs(attn_strided)[:, None, :])[:, 0]
    attn_both = jnp.concatenate([attn_local.reshape(tok_rows, head_dim), strided_home], axis=1)
    wo_both = jnp.concatenate([wo_local, wo_strided], axis=0)
    w_cols = wo_both
    mixed_cols, grad_rows = scatter_head(
        lax.dot_general(
            w_cols,
            attn_both,
            (((0,), (1,)), ((), ())),
            precision=HIGHEST,
            preferred_element_type=jnp.float32,
        ),
        gather_head(grad_out),
    )
    mixed = mixed_cols.T
    w_cols = wo_both
    grad_both = lax.dot_general(
        grad_rows.astype(jnp.float32),
        w_cols,
        (((1,), (1,)), ((), ())),
        precision=HIGHEST,
        preferred_element_type=jnp.float32,
    )
    grad_local = grad_both[:, :head_dim]
    grad_strided = to_strided(grad_both[:, head_dim:][:, None, :])[:, 0]
    dq_local, dk_local, dv_local = attend_backward(
        local_q, local_k, local_v, probs_local, attn_local, grad_local.reshape(local_layout)
    )
    dq_strided, dk_strided, dv_strided = attend_backward(
        strided_q, strided_k, strided_v, probs_strided, attn_strided, to_runs(grad_strided)
    )
    strided_grads = jnp.stack(
        [from_runs(dq_strided), from_runs(dk_strided), from_runs(dv_strided)], axis=1
    )
    grads_home = to_contiguous(strided_grads)
    grad_queries = dq_local.reshape(tok_rows, head_dim) + grads_home[:, 0]
    grad_keys = dk_local.reshape(tok_rows, head_dim) + grads_home[:, 1]
    grad_values = dv_local.reshape(tok_rows, head_dim) + grads_home[:, 2]
    return (mixed, grad_queries, grad_keys, grad_values)


def solution(mesh):
    seq_size, head_size = mesh.devices.shape
    zh = 2
    xs = 4
    view = jax.sharding.Mesh(mesh.devices.reshape(seq_size, zh, xs, head_size // (zh * xs)), ("seq",) + HEAD_AXES)
    return jax.shard_map(
        local,
        mesh=view,
        in_specs=(
            P("seq", HEAD_AXES),
            P("seq", HEAD_AXES),
            P("seq", HEAD_AXES),
            P(),
            P(HEAD_AXES, None),
            P(HEAD_AXES, None),
            P("seq", HEAD_AXES),
        ),
        out_specs=(P("seq", HEAD_AXES), P("seq", HEAD_AXES), P("seq", HEAD_AXES), P("seq", HEAD_AXES)),
        check_vma=False,
    )
```

```python
import jax
import jax.numpy as jnp
from jax import lax
from jax.sharding import PartitionSpec as P

HDIM = 128
BLOCK = 128
GROUP_BLK = 2
STRIDE = 128


HIGHEST = lax.Precision.HIGHEST


HEAD_AXES = ("zh", "x", "y")


def swapped(x, axis, distance):
    return lax.ppermute(x, axis, [(i, i ^ 1 << distance) for i in range(lax.axis_size(axis))])


def pair_sum(partial_value):
    return partial_value + swapped(partial_value, "y", 0)


def head_index():
    return (lax.axis_index("zh") * lax.axis_size("x") + lax.axis_index("x")) * lax.axis_size("y") + lax.axis_index("y")


def scatter_head(partial_value, companion):
    sizes = [lax.axis_size(a) for a in HEAD_AXES]
    rows, cols = partial_value.shape
    block = rows // (sizes[0] * sizes[1] * sizes[2])
    parts = partial_value.reshape(*sizes, block, cols)
    parts = lax.all_to_all(parts, "x", 1, 1, tiled=True).sum(1)
    for dim in (1, 0):
        parts = lax.all_to_all(parts, HEAD_AXES[2 * dim], dim, dim, tiled=True).sum(dim)
    return lax.optimization_barrier((parts, companion))


def gather_head(piece):
    return lax.all_gather(piece, HEAD_AXES, axis=1, tiled=True)


def attend_forward(query_part, key_part, value_part, allowed):
    scale_factor = HDIM ** (-0.5)
    partial_value = jnp.einsum("bqhd,bkhd->bhqk", query_part, key_part, precision=HIGHEST)
    scores = pair_sum(partial_value) * scale_factor
    row_max = jnp.max(jnp.where(allowed, scores, -jnp.inf), axis=-1, keepdims=True)
    weights = jnp.where(allowed, jnp.exp(scores - row_max), 0.0)
    probs = weights / jnp.sum(weights, axis=-1, keepdims=True)
    attended = jnp.einsum("bhqk,bkhd->bqhd", probs, value_part, precision=HIGHEST)
    return (attended, probs)


def attend_backward(query_part, key_part, value_part, probs, attended, incoming):
    scale_factor = HDIM ** (-0.5)
    dprobs_part = jnp.einsum("bqhd,bkhd->bhqk", incoming, value_part, precision=HIGHEST)
    delta_part = jnp.transpose(jnp.sum(incoming * attended, axis=-1), (0, 2, 1))[..., None]
    joined = pair_sum(jnp.concatenate([dprobs_part, delta_part], axis=-1))
    dprobs = joined[..., :-1]
    row_delta = joined[..., -1:]
    dscores = probs * (dprobs - row_delta)
    grad_query = jnp.einsum("bhqk,bkhd->bqhd", dscores, key_part, precision=HIGHEST) * scale_factor
    grad_key = jnp.einsum("bhqk,bqhd->bkhd", dscores, query_part, precision=HIGHEST) * scale_factor
    grad_value = jnp.einsum("bhqk,bqhd->bkhd", probs, incoming, precision=HIGHEST)
    return (grad_query, grad_key, grad_value)


def to_strided(stacked):
    seq_devices = lax.axis_size("seq")
    tok_rows, members, head_dim = stacked.shape
    layout = stacked.reshape(tok_rows // seq_devices, seq_devices, members, head_dim)
    moved = lax.all_to_all(layout, "seq", split_axis=1, concat_axis=0, tiled=True)
    return moved.reshape(tok_rows, members, head_dim)


def to_contiguous(stacked):
    seq_devices = lax.axis_size("seq")
    tok_rows, members, head_dim = stacked.shape
    layout = stacked.reshape(seq_devices, tok_rows // seq_devices, 1, members, head_dim)
    moved = lax.all_to_all(layout, "seq", split_axis=0, concat_axis=2, tiled=True)
    return moved.reshape(tok_rows, members, head_dim)


def local(queries, keys, values, local_span, wo_local, wo_strided, grad_out):
    tok_rows, head_dim = queries.shape
    seq_devices = lax.axis_size("seq")
    per_run = STRIDE // seq_devices
    runs_here = tok_rows // per_run
    group_len = GROUP_BLK * BLOCK
    local_layout = (tok_rows // group_len, group_len, 1, head_dim)
    own_span = local_span[head_index() // 2]
    stacked = jnp.stack([queries, keys, values], axis=1)
    spread = to_strided(stacked)
    local_q = queries.reshape(local_layout)
    local_k = keys.reshape(local_layout)
    local_v = values.reshape(local_layout)
    position = jnp.arange(group_len)
    block_of = position // BLOCK
    causal = position[None, :] <= position[:, None]
    reach = block_of[:, None] - block_of[None, :] < own_span
    allowed_local = (causal & reach)[None, None]
    attn_local, probs_local = attend_forward(local_q, local_k, local_v, allowed_local)

    def to_runs(matrix):
        return matrix.reshape(runs_here, per_run, 1, head_dim).transpose(1, 0, 2, 3)

    def from_runs(arranged):
        return arranged.transpose(1, 0, 2, 3).reshape(tok_rows, head_dim)

    strided_q = to_runs(spread[:, 0])
    strided_k = to_runs(spread[:, 1])
    strided_v = to_runs(spread[:, 2])
    order = jnp.arange(runs_here)
    allowed_strided = (order[None, :] <= order[:, None])[None, None]
    attn_strided, probs_strided = attend_forward(strided_q, strided_k, strided_v, allowed_strided)
    strided_home = to_contiguous(from_runs(attn_strided)[:, None, :])[:, 0]
    attn_both = jnp.concatenate([attn_local.reshape(tok_rows, head_dim), strided_home], axis=1)
    wo_both = jnp.concatenate([wo_local, wo_strided], axis=0)
    w_cols = wo_both
    mixed_cols, grad_rows = scatter_head(
        lax.dot_general(
            w_cols,
            attn_both,
            (((0,), (1,)), ((), ())),
            precision=HIGHEST,
            preferred_element_type=jnp.float32,
        ),
        gather_head(grad_out),
    )
    mixed = mixed_cols.T
    w_cols = wo_both
    grad_both = lax.dot_general(
        grad_rows.astype(jnp.float32),
        w_cols,
        (((1,), (1,)), ((), ())),
        precision=HIGHEST,
        preferred_element_type=jnp.float32,
    )
    grad_local = grad_both[:, :head_dim]
    grad_strided = to_strided(grad_both[:, head_dim:][:, None, :])[:, 0]
    dq_local, dk_local, dv_local = attend_backward(
        local_q, local_k, local_v, probs_local, attn_local, grad_local.reshape(local_layout)
    )
    dq_strided, dk_strided, dv_strided = attend_backward(
        strided_q, strided_k, strided_v, probs_strided, attn_strided, to_runs(grad_strided)
    )
    strided_grads = jnp.stack(
        [from_runs(dq_strided), from_runs(dk_strided), from_runs(dv_strided)], axis=1
    )
    grads_home = to_contiguous(strided_grads)
    grad_queries = dq_local.reshape(tok_rows, head_dim) + grads_home[:, 0]
    grad_keys = dk_local.reshape(tok_rows, head_dim) + grads_home[:, 1]
    grad_values = dv_local.reshape(tok_rows, head_dim) + grads_home[:, 2]
    return (mixed, grad_queries, grad_keys, grad_values)


def solution(mesh):
    seq_size, head_size = mesh.devices.shape
    zh = 2
    xs = 4
    view = jax.sharding.Mesh(mesh.devices.reshape(seq_size, zh, xs, head_size // (zh * xs)), ("seq",) + HEAD_AXES)
    return jax.shard_map(
        local,
        mesh=view,
        in_specs=(
            P("seq", HEAD_AXES),
            P("seq", HEAD_AXES),
            P("seq", HEAD_AXES),
            P(),
            P(HEAD_AXES, None),
            P(HEAD_AXES, None),
            P("seq", HEAD_AXES),
        ),
        out_specs=(P("seq", HEAD_AXES), P("seq", HEAD_AXES), P("seq", HEAD_AXES), P("seq", HEAD_AXES)),
        check_vma=False,
    )
```

```python
import jax
import jax.numpy as jnp
from jax import lax
from jax.sharding import PartitionSpec as P

HDIM = 128
BLOCK = 128
GROUP_BLK = 2
STRIDE = 128


HIGHEST = lax.Precision.HIGHEST


HEAD_AXES = ("zh", "x", "y")


def swapped(x, axis, distance):
    return lax.ppermute(x, axis, [(i, i ^ 1 << distance) for i in range(lax.axis_size(axis))])


def pair_sum(partial_value):
    return partial_value + swapped(partial_value, "y", 0)


def head_index():
    return (lax.axis_index("zh") * lax.axis_size("x") + lax.axis_index("x")) * lax.axis_size("y") + lax.axis_index("y")


def scatter_head(partial_value, companion):
    sizes = [lax.axis_size(a) for a in HEAD_AXES]
    rows, cols = partial_value.shape
    block = rows // (sizes[0] * sizes[1] * sizes[2])
    parts = partial_value.reshape(*sizes, block, cols)
    parts = lax.all_to_all(parts, "x", 1, 1, tiled=True).sum(1)
    parts, companion = lax.optimization_barrier((parts, companion))
    for dim in (1, 0):
        parts = lax.all_to_all(parts, HEAD_AXES[2 * dim], dim, dim, tiled=True).sum(dim)
    return parts, companion


def gather_head(piece):
    rows, cols = piece.shape
    stacked = piece
    for axis in ("zh", "y", "x"):
        count = lax.axis_size(axis)
        copies = jnp.broadcast_to(stacked[None], (count,) + stacked.shape)
        stacked = lax.all_to_all(copies, axis, 0, 0, tiled=True)
    order = stacked.reshape(stacked.shape[:3] + (rows, cols)).transpose(3, 2, 0, 1, 4)
    return order.reshape(rows, -1)


def attend_forward(query_part, key_part, value_part, allowed):
    scale_factor = HDIM ** (-0.5)
    partial_value = jnp.einsum("bqhd,bkhd->bhqk", query_part, key_part, precision=HIGHEST)
    scores = pair_sum(partial_value) * scale_factor
    row_max = jnp.max(jnp.where(allowed, scores, -jnp.inf), axis=-1, keepdims=True)
    weights = jnp.where(allowed, jnp.exp(scores - row_max), 0.0)
    probs = weights / jnp.sum(weights, axis=-1, keepdims=True)
    attended = jnp.einsum("bhqk,bkhd->bqhd", probs, value_part, precision=HIGHEST)
    return (attended, probs)


def attend_backward(query_part, key_part, value_part, probs, attended, incoming):
    scale_factor = HDIM ** (-0.5)
    dprobs_part = jnp.einsum("bqhd,bkhd->bhqk", incoming, value_part, precision=HIGHEST)
    delta_part = jnp.transpose(jnp.sum(incoming * attended, axis=-1), (0, 2, 1))[..., None]
    joined = pair_sum(jnp.concatenate([dprobs_part, delta_part], axis=-1))
    dprobs = joined[..., :-1]
    row_delta = joined[..., -1:]
    dscores = probs * (dprobs - row_delta)
    grad_query = jnp.einsum("bhqk,bkhd->bqhd", dscores, key_part, precision=HIGHEST) * scale_factor
    grad_key = jnp.einsum("bhqk,bqhd->bkhd", dscores, query_part, precision=HIGHEST) * scale_factor
    grad_value = jnp.einsum("bhqk,bqhd->bkhd", probs, incoming, precision=HIGHEST)
    return (grad_query, grad_key, grad_value)


def to_strided(stacked):
    seq_devices = lax.axis_size("seq")
    tok_rows, members, head_dim = stacked.shape
    layout = stacked.reshape(tok_rows // seq_devices, seq_devices, members, head_dim)
    moved = lax.all_to_all(layout, "seq", split_axis=1, concat_axis=0, tiled=True)
    return moved.reshape(tok_rows, members, head_dim)


def to_contiguous(stacked):
    seq_devices = lax.axis_size("seq")
    tok_rows, members, head_dim = stacked.shape
    layout = stacked.reshape(seq_devices, tok_rows // seq_devices, 1, members, head_dim)
    moved = lax.all_to_all(layout, "seq", split_axis=0, concat_axis=2, tiled=True)
    return moved.reshape(tok_rows, members, head_dim)


def local(queries, keys, values, local_span, wo_local, wo_strided, grad_out):
    tok_rows, head_dim = queries.shape
    seq_devices = lax.axis_size("seq")
    per_run = STRIDE // seq_devices
    runs_here = tok_rows // per_run
    group_len = GROUP_BLK * BLOCK
    local_layout = (tok_rows // group_len, group_len, 1, head_dim)
    own_span = local_span[head_index() // 2]
    stacked = jnp.stack([queries, keys, values], axis=1)
    spread = to_strided(stacked)
    local_q = queries.reshape(local_layout)
    local_k = keys.reshape(local_layout)
    local_v = values.reshape(local_layout)
    position = jnp.arange(group_len)
    block_of = position // BLOCK
    causal = position[None, :] <= position[:, None]
    reach = block_of[:, None] - block_of[None, :] < own_span
    allowed_local = (causal & reach)[None, None]
    attn_local, probs_local = attend_forward(local_q, local_k, local_v, allowed_local)

    def to_runs(matrix):
        return matrix.reshape(runs_here, per_run, 1, head_dim).transpose(1, 0, 2, 3)

    def from_runs(arranged):
        return arranged.transpose(1, 0, 2, 3).reshape(tok_rows, head_dim)

    strided_q = to_runs(spread[:, 0])
    strided_k = to_runs(spread[:, 1])
    strided_v = to_runs(spread[:, 2])
    order = jnp.arange(runs_here)
    allowed_strided = (order[None, :] <= order[:, None])[None, None]
    attn_strided, probs_strided = attend_forward(strided_q, strided_k, strided_v, allowed_strided)
    strided_home = to_contiguous(from_runs(attn_strided)[:, None, :])[:, 0]
    attn_both = jnp.concatenate([attn_local.reshape(tok_rows, head_dim), strided_home], axis=1)
    wo_both = jnp.concatenate([wo_local, wo_strided], axis=0)
    w_cols = wo_both
    mixed_cols, grad_rows = scatter_head(
        lax.dot_general(
            w_cols,
            attn_both,
            (((0,), (1,)), ((), ())),
            precision=HIGHEST,
            preferred_element_type=jnp.float32,
        ),
        gather_head(grad_out),
    )
    mixed = mixed_cols.T
    w_cols = wo_both
    grad_both = lax.dot_general(
        grad_rows.astype(jnp.float32),
        w_cols,
        (((1,), (1,)), ((), ())),
        precision=HIGHEST,
        preferred_element_type=jnp.float32,
    )
    grad_local = grad_both[:, :head_dim]
    grad_strided = to_strided(grad_both[:, head_dim:][:, None, :])[:, 0]
    dq_local, dk_local, dv_local = attend_backward(
        local_q, local_k, local_v, probs_local, attn_local, grad_local.reshape(local_layout)
    )
    dq_strided, dk_strided, dv_strided = attend_backward(
        strided_q, strided_k, strided_v, probs_strided, attn_strided, to_runs(grad_strided)
    )
    strided_grads = jnp.stack(
        [from_runs(dq_strided), from_runs(dk_strided), from_runs(dv_strided)], axis=1
    )
    grads_home = to_contiguous(strided_grads)
    grad_queries = dq_local.reshape(tok_rows, head_dim) + grads_home[:, 0]
    grad_keys = dk_local.reshape(tok_rows, head_dim) + grads_home[:, 1]
    grad_values = dv_local.reshape(tok_rows, head_dim) + grads_home[:, 2]
    return (mixed, grad_queries, grad_keys, grad_values)


def solution(mesh):
    seq_size, head_size = mesh.devices.shape
    zh = 2
    xs = 4
    view = jax.sharding.Mesh(mesh.devices.reshape(seq_size, zh, xs, head_size // (zh * xs)), ("seq",) + HEAD_AXES)
    return jax.shard_map(
        local,
        mesh=view,
        in_specs=(
            P("seq", HEAD_AXES),
            P("seq", HEAD_AXES),
            P("seq", HEAD_AXES),
            P(),
            P(HEAD_AXES, None),
            P(HEAD_AXES, None),
            P("seq", HEAD_AXES),
        ),
        out_specs=(P("seq", HEAD_AXES), P("seq", HEAD_AXES), P("seq", HEAD_AXES), P("seq", HEAD_AXES)),
        check_vma=False,
    )
```

```python
import jax
import jax.numpy as jnp
from jax import lax
from jax.sharding import PartitionSpec as P

HDIM = 128
BLOCK = 128
GROUP_BLK = 2
STRIDE = 128


HIGHEST = lax.Precision.HIGHEST


HEAD_AXES = ("zh", "x", "y")


def swapped(x, axis, distance):
    return lax.ppermute(x, axis, [(i, i ^ 1 << distance) for i in range(lax.axis_size(axis))])


def pair_sum(partial_value):
    return partial_value + swapped(partial_value, "y", 0)


def head_index():
    return (lax.axis_index("zh") * lax.axis_size("x") + lax.axis_index("x")) * lax.axis_size("y") + lax.axis_index("y")


def scatter_head(partial_value, companion):
    sizes = [lax.axis_size(a) for a in HEAD_AXES]
    rows, cols = partial_value.shape
    block = rows // (sizes[0] * sizes[1] * sizes[2])
    parts = partial_value.reshape(*sizes, block, cols)
    parts = lax.all_to_all(parts, "x", 1, 1, tiled=True).sum(1)
    for dim in (1, 0):
        parts = lax.all_to_all(parts, HEAD_AXES[2 * dim], dim, dim, tiled=True).sum(dim)
    return parts, companion


def gather_head(piece):
    rows, cols = piece.shape
    stacked = piece
    for axis in ("zh", "y", "x"):
        count = lax.axis_size(axis)
        copies = jnp.broadcast_to(stacked[None], (count,) + stacked.shape)
        stacked = lax.all_to_all(copies, axis, 0, 0, tiled=True)
    order = stacked.reshape(stacked.shape[:3] + (rows, cols)).transpose(3, 2, 0, 1, 4)
    return order.reshape(rows, -1)


def attend_forward(query_part, key_part, value_part, allowed):
    scale_factor = HDIM ** (-0.5)
    partial_value = jnp.einsum("bqhd,bkhd->bhqk", query_part, key_part, precision=HIGHEST)
    scores = pair_sum(partial_value) * scale_factor
    row_max = jnp.max(jnp.where(allowed, scores, -jnp.inf), axis=-1, keepdims=True)
    weights = jnp.where(allowed, jnp.exp(scores - row_max), 0.0)
    probs = weights / jnp.sum(weights, axis=-1, keepdims=True)
    attended = jnp.einsum("bhqk,bkhd->bqhd", probs, value_part, precision=HIGHEST)
    return (attended, probs)


def attend_backward(query_part, key_part, value_part, probs, attended, incoming):
    scale_factor = HDIM ** (-0.5)
    dprobs_part = jnp.einsum("bqhd,bkhd->bhqk", incoming, value_part, precision=HIGHEST)
    delta_part = jnp.transpose(jnp.sum(incoming * attended, axis=-1), (0, 2, 1))[..., None]
    joined = pair_sum(jnp.concatenate([dprobs_part, delta_part], axis=-1))
    dprobs = joined[..., :-1]
    row_delta = joined[..., -1:]
    dscores = probs * (dprobs - row_delta)
    grad_query = jnp.einsum("bhqk,bkhd->bqhd", dscores, key_part, precision=HIGHEST) * scale_factor
    grad_key = jnp.einsum("bhqk,bqhd->bkhd", dscores, query_part, precision=HIGHEST) * scale_factor
    grad_value = jnp.einsum("bhqk,bqhd->bkhd", probs, incoming, precision=HIGHEST)
    return (grad_query, grad_key, grad_value)


def to_strided(stacked):
    seq_devices = lax.axis_size("seq")
    tok_rows, members, head_dim = stacked.shape
    layout = stacked.reshape(tok_rows // seq_devices, seq_devices, members, head_dim)
    moved = lax.all_to_all(layout, "seq", split_axis=1, concat_axis=0, tiled=True)
    return moved.reshape(tok_rows, members, head_dim)


def to_contiguous(stacked):
    seq_devices = lax.axis_size("seq")
    tok_rows, members, head_dim = stacked.shape
    layout = stacked.reshape(seq_devices, tok_rows // seq_devices, 1, members, head_dim)
    moved = lax.all_to_all(layout, "seq", split_axis=0, concat_axis=2, tiled=True)
    return moved.reshape(tok_rows, members, head_dim)


def local(queries, keys, values, local_span, wo_local, wo_strided, grad_out):
    tok_rows, head_dim = queries.shape
    seq_devices = lax.axis_size("seq")
    per_run = STRIDE // seq_devices
    runs_here = tok_rows // per_run
    group_len = GROUP_BLK * BLOCK
    local_layout = (tok_rows // group_len, group_len, 1, head_dim)
    own_span = local_span[head_index() // 2]
    stacked = jnp.stack([queries, keys, values], axis=1)
    spread = to_strided(stacked)
    local_q = queries.reshape(local_layout)
    local_k = keys.reshape(local_layout)
    local_v = values.reshape(local_layout)
    position = jnp.arange(group_len)
    block_of = position // BLOCK
    causal = position[None, :] <= position[:, None]
    reach = block_of[:, None] - block_of[None, :] < own_span
    allowed_local = (causal & reach)[None, None]
    attn_local, probs_local = attend_forward(local_q, local_k, local_v, allowed_local)

    def to_runs(matrix):
        return matrix.reshape(runs_here, per_run, 1, head_dim).transpose(1, 0, 2, 3)

    def from_runs(arranged):
        return arranged.transpose(1, 0, 2, 3).reshape(tok_rows, head_dim)

    strided_q = to_runs(spread[:, 0])
    strided_k = to_runs(spread[:, 1])
    strided_v = to_runs(spread[:, 2])
    order = jnp.arange(runs_here)
    allowed_strided = (order[None, :] <= order[:, None])[None, None]
    attn_strided, probs_strided = attend_forward(strided_q, strided_k, strided_v, allowed_strided)
    strided_home = to_contiguous(from_runs(attn_strided)[:, None, :])[:, 0]
    attn_both = jnp.concatenate([attn_local.reshape(tok_rows, head_dim), strided_home], axis=1)
    wo_both = jnp.concatenate([wo_local, wo_strided], axis=0)
    w_cols = wo_both
    mixed_cols, grad_rows = scatter_head(
        lax.dot_general(
            w_cols,
            attn_both,
            (((0,), (1,)), ((), ())),
            precision=HIGHEST,
            preferred_element_type=jnp.float32,
        ),
        gather_head(grad_out),
    )
    mixed = mixed_cols.T
    w_cols = wo_both
    grad_both = lax.dot_general(
        grad_rows.astype(jnp.float32),
        w_cols,
        (((1,), (1,)), ((), ())),
        precision=HIGHEST,
        preferred_element_type=jnp.float32,
    )
    grad_local = grad_both[:, :head_dim]
    grad_strided = to_strided(grad_both[:, head_dim:][:, None, :])[:, 0]
    dq_local, dk_local, dv_local = attend_backward(
        local_q, local_k, local_v, probs_local, attn_local, grad_local.reshape(local_layout)
    )
    dq_strided, dk_strided, dv_strided = attend_backward(
        strided_q, strided_k, strided_v, probs_strided, attn_strided, to_runs(grad_strided)
    )
    strided_grads = jnp.stack(
        [from_runs(dq_strided), from_runs(dk_strided), from_runs(dv_strided)], axis=1
    )
    grads_home = to_contiguous(strided_grads)
    grad_queries = dq_local.reshape(tok_rows, head_dim) + grads_home[:, 0]
    grad_keys = dk_local.reshape(tok_rows, head_dim) + grads_home[:, 1]
    grad_values = dv_local.reshape(tok_rows, head_dim) + grads_home[:, 2]
    return (mixed, grad_queries, grad_keys, grad_values)


def solution(mesh):
    seq_size, head_size = mesh.devices.shape
    zh = 2
    xs = 4
    view = jax.sharding.Mesh(mesh.devices.reshape(seq_size, zh, xs, head_size // (zh * xs)), ("seq",) + HEAD_AXES)
    return jax.shard_map(
        local,
        mesh=view,
        in_specs=(
            P("seq", HEAD_AXES),
            P("seq", HEAD_AXES),
            P("seq", HEAD_AXES),
            P(),
            P(HEAD_AXES, None),
            P(HEAD_AXES, None),
            P("seq", HEAD_AXES),
        ),
        out_specs=(P("seq", HEAD_AXES), P("seq", HEAD_AXES), P("seq", HEAD_AXES), P("seq", HEAD_AXES)),
        check_vma=False,
    )
```

```python
import jax
import jax.numpy as jnp
from jax import lax
from jax.sharding import PartitionSpec as P

HDIM = 128
BLOCK = 128
GROUP_BLK = 2
STRIDE = 128


HIGHEST = lax.Precision.HIGHEST


HEAD_AXES = ("zh", "x", "y")


def swapped(x, axis, distance):
    return lax.ppermute(x, axis, [(i, i ^ 1 << distance) for i in range(lax.axis_size(axis))])


def pair_sum(partial_value):
    return partial_value + swapped(partial_value, "y", 0)


def head_index():
    return (lax.axis_index("zh") * lax.axis_size("x") + lax.axis_index("x")) * lax.axis_size("y") + lax.axis_index("y")


def scatter_head(partial_value, companion):
    sizes = [lax.axis_size(a) for a in HEAD_AXES]
    rows, cols = partial_value.shape
    block = rows // (sizes[0] * sizes[1] * sizes[2])
    parts = partial_value.reshape(*sizes, block, cols)
    parts = lax.all_to_all(parts, "x", 1, 1, tiled=True).sum(1)
    for dim in (1, 0):
        parts = lax.all_to_all(parts, HEAD_AXES[2 * dim], dim, dim, tiled=True).sum(dim)
    return parts, companion


def gather_head(piece):
    rows, cols = piece.shape
    stacked = piece
    for axis in (("zh", "y"), "x"):
        count = lax.axis_size(axis)
        copies = jnp.broadcast_to(stacked[None], (count,) + stacked.shape)
        stacked = lax.all_to_all(copies, axis, 0, 0, tiled=True)
    zh, ys = lax.axis_size("zh"), lax.axis_size("y")
    order = stacked.reshape((stacked.shape[0], zh, ys, rows, cols)).transpose(3, 1, 0, 2, 4)
    return order.reshape(rows, -1)


def attend_forward(query_part, key_part, value_part, allowed):
    scale_factor = HDIM ** (-0.5)
    partial_value = jnp.einsum("bqhd,bkhd->bhqk", query_part, key_part, precision=HIGHEST)
    scores = pair_sum(partial_value) * scale_factor
    row_max = jnp.max(jnp.where(allowed, scores, -jnp.inf), axis=-1, keepdims=True)
    weights = jnp.where(allowed, jnp.exp(scores - row_max), 0.0)
    probs = weights / jnp.sum(weights, axis=-1, keepdims=True)
    attended = jnp.einsum("bhqk,bkhd->bqhd", probs, value_part, precision=HIGHEST)
    return (attended, probs)


def attend_backward(query_part, key_part, value_part, probs, attended, incoming):
    scale_factor = HDIM ** (-0.5)
    dprobs_part = jnp.einsum("bqhd,bkhd->bhqk", incoming, value_part, precision=HIGHEST)
    delta_part = jnp.transpose(jnp.sum(incoming * attended, axis=-1), (0, 2, 1))[..., None]
    joined = pair_sum(jnp.concatenate([dprobs_part, delta_part], axis=-1))
    dprobs = joined[..., :-1]
    row_delta = joined[..., -1:]
    dscores = probs * (dprobs - row_delta)
    grad_query = jnp.einsum("bhqk,bkhd->bqhd", dscores, key_part, precision=HIGHEST) * scale_factor
    grad_key = jnp.einsum("bhqk,bqhd->bkhd", dscores, query_part, precision=HIGHEST) * scale_factor
    grad_value = jnp.einsum("bhqk,bqhd->bkhd", probs, incoming, precision=HIGHEST)
    return (grad_query, grad_key, grad_value)


def to_strided(stacked):
    seq_devices = lax.axis_size("seq")
    tok_rows, members, head_dim = stacked.shape
    layout = stacked.reshape(tok_rows // seq_devices, seq_devices, members, head_dim)
    moved = lax.all_to_all(layout, "seq", split_axis=1, concat_axis=0, tiled=True)
    return moved.reshape(tok_rows, members, head_dim)


def to_contiguous(stacked):
    seq_devices = lax.axis_size("seq")
    tok_rows, members, head_dim = stacked.shape
    layout = stacked.reshape(seq_devices, tok_rows // seq_devices, 1, members, head_dim)
    moved = lax.all_to_all(layout, "seq", split_axis=0, concat_axis=2, tiled=True)
    return moved.reshape(tok_rows, members, head_dim)


def local(queries, keys, values, local_span, wo_local, wo_strided, grad_out):
    tok_rows, head_dim = queries.shape
    seq_devices = lax.axis_size("seq")
    per_run = STRIDE // seq_devices
    runs_here = tok_rows // per_run
    group_len = GROUP_BLK * BLOCK
    local_layout = (tok_rows // group_len, group_len, 1, head_dim)
    own_span = local_span[head_index() // 2]
    stacked = jnp.stack([queries, keys, values], axis=1)
    spread = to_strided(stacked)
    local_q = queries.reshape(local_layout)
    local_k = keys.reshape(local_layout)
    local_v = values.reshape(local_layout)
    position = jnp.arange(group_len)
    block_of = position // BLOCK
    causal = position[None, :] <= position[:, None]
    reach = block_of[:, None] - block_of[None, :] < own_span
    allowed_local = (causal & reach)[None, None]
    attn_local, probs_local = attend_forward(local_q, local_k, local_v, allowed_local)

    def to_runs(matrix):
        return matrix.reshape(runs_here, per_run, 1, head_dim).transpose(1, 0, 2, 3)

    def from_runs(arranged):
        return arranged.transpose(1, 0, 2, 3).reshape(tok_rows, head_dim)

    strided_q = to_runs(spread[:, 0])
    strided_k = to_runs(spread[:, 1])
    strided_v = to_runs(spread[:, 2])
    order = jnp.arange(runs_here)
    allowed_strided = (order[None, :] <= order[:, None])[None, None]
    attn_strided, probs_strided = attend_forward(strided_q, strided_k, strided_v, allowed_strided)
    strided_home = to_contiguous(from_runs(attn_strided)[:, None, :])[:, 0]
    attn_both = jnp.concatenate([attn_local.reshape(tok_rows, head_dim), strided_home], axis=1)
    wo_both = jnp.concatenate([wo_local, wo_strided], axis=0)
    w_cols = wo_both
    mixed_cols, grad_rows = scatter_head(
        lax.dot_general(
            w_cols,
            attn_both,
            (((0,), (1,)), ((), ())),
            precision=HIGHEST,
            preferred_element_type=jnp.float32,
        ),
        gather_head(grad_out),
    )
    mixed = mixed_cols.T
    w_cols = wo_both
    grad_both = lax.dot_general(
        grad_rows.astype(jnp.float32),
        w_cols,
        (((1,), (1,)), ((), ())),
        precision=HIGHEST,
        preferred_element_type=jnp.float32,
    )
    grad_local = grad_both[:, :head_dim]
    grad_strided = to_strided(grad_both[:, head_dim:][:, None, :])[:, 0]
    dq_local, dk_local, dv_local = attend_backward(
        local_q, local_k, local_v, probs_local, attn_local, grad_local.reshape(local_layout)
    )
    dq_strided, dk_strided, dv_strided = attend_backward(
        strided_q, strided_k, strided_v, probs_strided, attn_strided, to_runs(grad_strided)
    )
    strided_grads = jnp.stack(
        [from_runs(dq_strided), from_runs(dk_strided), from_runs(dv_strided)], axis=1
    )
    grads_home = to_contiguous(strided_grads)
    grad_queries = dq_local.reshape(tok_rows, head_dim) + grads_home[:, 0]
    grad_keys = dk_local.reshape(tok_rows, head_dim) + grads_home[:, 1]
    grad_values = dv_local.reshape(tok_rows, head_dim) + grads_home[:, 2]
    return (mixed, grad_queries, grad_keys, grad_values)


def solution(mesh):
    seq_size, head_size = mesh.devices.shape
    zh = 2
    xs = 4
    view = jax.sharding.Mesh(mesh.devices.reshape(seq_size, zh, xs, head_size // (zh * xs)), ("seq",) + HEAD_AXES)
    return jax.shard_map(
        local,
        mesh=view,
        in_specs=(
            P("seq", HEAD_AXES),
            P("seq", HEAD_AXES),
            P("seq", HEAD_AXES),
            P(),
            P(HEAD_AXES, None),
            P(HEAD_AXES, None),
            P("seq", HEAD_AXES),
        ),
        out_specs=(P("seq", HEAD_AXES), P("seq", HEAD_AXES), P("seq", HEAD_AXES), P("seq", HEAD_AXES)),
        check_vma=False,
    )
```

```python
import jax
import jax.numpy as jnp
from jax import lax
from jax.sharding import PartitionSpec as P

HDIM = 128
BLOCK = 128
GROUP_BLK = 2
STRIDE = 128


HIGHEST = lax.Precision.HIGHEST


HEAD_AXES = ("zh", "x", "y")


def swapped(x, axis, distance):
    return lax.ppermute(x, axis, [(i, i ^ 1 << distance) for i in range(lax.axis_size(axis))])


def pair_sum(partial_value):
    return partial_value + swapped(partial_value, "y", 0)


def head_index():
    return (lax.axis_index("zh") * lax.axis_size("x") + lax.axis_index("x")) * lax.axis_size("y") + lax.axis_index("y")


def scatter_head(partial_value, companion):
    sizes = [lax.axis_size(a) for a in HEAD_AXES]
    rows, cols = partial_value.shape
    block = rows // (sizes[0] * sizes[1] * sizes[2])
    parts = partial_value.reshape(*sizes, block, cols)
    parts = lax.all_to_all(parts, "x", 1, 1, tiled=True).sum(1)
    parts = lax.all_to_all(parts, "y", 1, 1, tiled=True).sum(1)
    own = lax.axis_index("zh")
    kept = lax.dynamic_index_in_dim(parts, own, 0, keepdims=False)
    sent = lax.dynamic_index_in_dim(parts, 1 - own, 0, keepdims=False)
    return kept + swapped(sent, "zh", 0), companion


def gather_head(piece):
    rows, cols = piece.shape
    other = swapped(piece, "zh", 0)
    first = lax.axis_index("zh") == 0
    stacked = jnp.stack([jnp.where(first, piece, other), jnp.where(first, other, piece)])
    for axis in ("y", "x"):
        count = lax.axis_size(axis)
        copies = jnp.broadcast_to(stacked[None], (count,) + stacked.shape)
        stacked = lax.all_to_all(copies, axis, 0, 0, tiled=True)
    order = stacked.reshape(stacked.shape[:3] + (rows, cols)).transpose(3, 2, 0, 1, 4)
    return order.reshape(rows, -1)


def attend_forward(query_part, key_part, value_part, allowed):
    scale_factor = HDIM ** (-0.5)
    partial_value = jnp.einsum("bqhd,bkhd->bhqk", query_part, key_part, precision=HIGHEST)
    scores = pair_sum(partial_value) * scale_factor
    row_max = jnp.max(jnp.where(allowed, scores, -jnp.inf), axis=-1, keepdims=True)
    weights = jnp.where(allowed, jnp.exp(scores - row_max), 0.0)
    probs = weights / jnp.sum(weights, axis=-1, keepdims=True)
    attended = jnp.einsum("bhqk,bkhd->bqhd", probs, value_part, precision=HIGHEST)
    return (attended, probs)


def attend_backward(query_part, key_part, value_part, probs, attended, incoming):
    scale_factor = HDIM ** (-0.5)
    dprobs_part = jnp.einsum("bqhd,bkhd->bhqk", incoming, value_part, precision=HIGHEST)
    delta_part = jnp.transpose(jnp.sum(incoming * attended, axis=-1), (0, 2, 1))[..., None]
    joined = pair_sum(jnp.concatenate([dprobs_part, delta_part], axis=-1))
    dprobs = joined[..., :-1]
    row_delta = joined[..., -1:]
    dscores = probs * (dprobs - row_delta)
    grad_query = jnp.einsum("bhqk,bkhd->bqhd", dscores, key_part, precision=HIGHEST) * scale_factor
    grad_key = jnp.einsum("bhqk,bqhd->bkhd", dscores, query_part, precision=HIGHEST) * scale_factor
    grad_value = jnp.einsum("bhqk,bqhd->bkhd", probs, incoming, precision=HIGHEST)
    return (grad_query, grad_key, grad_value)


def to_strided(stacked):
    seq_devices = lax.axis_size("seq")
    tok_rows, members, head_dim = stacked.shape
    layout = stacked.reshape(tok_rows // seq_devices, seq_devices, members, head_dim)
    moved = lax.all_to_all(layout, "seq", split_axis=1, concat_axis=0, tiled=True)
    return moved.reshape(tok_rows, members, head_dim)


def to_contiguous(stacked):
    seq_devices = lax.axis_size("seq")
    tok_rows, members, head_dim = stacked.shape
    layout = stacked.reshape(seq_devices, tok_rows // seq_devices, 1, members, head_dim)
    moved = lax.all_to_all(layout, "seq", split_axis=0, concat_axis=2, tiled=True)
    return moved.reshape(tok_rows, members, head_dim)


def local(queries, keys, values, local_span, wo_local, wo_strided, grad_out):
    tok_rows, head_dim = queries.shape
    seq_devices = lax.axis_size("seq")
    per_run = STRIDE // seq_devices
    runs_here = tok_rows // per_run
    group_len = GROUP_BLK * BLOCK
    local_layout = (tok_rows // group_len, group_len, 1, head_dim)
    own_span = local_span[head_index() // 2]
    stacked = jnp.stack([queries, keys, values], axis=1)
    spread = to_strided(stacked)
    local_q = queries.reshape(local_layout)
    local_k = keys.reshape(local_layout)
    local_v = values.reshape(local_layout)
    position = jnp.arange(group_len)
    block_of = position // BLOCK
    causal = position[None, :] <= position[:, None]
    reach = block_of[:, None] - block_of[None, :] < own_span
    allowed_local = (causal & reach)[None, None]
    attn_local, probs_local = attend_forward(local_q, local_k, local_v, allowed_local)

    def to_runs(matrix):
        return matrix.reshape(runs_here, per_run, 1, head_dim).transpose(1, 0, 2, 3)

    def from_runs(arranged):
        return arranged.transpose(1, 0, 2, 3).reshape(tok_rows, head_dim)

    strided_q = to_runs(spread[:, 0])
    strided_k = to_runs(spread[:, 1])
    strided_v = to_runs(spread[:, 2])
    order = jnp.arange(runs_here)
    allowed_strided = (order[None, :] <= order[:, None])[None, None]
    attn_strided, probs_strided = attend_forward(strided_q, strided_k, strided_v, allowed_strided)
    strided_home = to_contiguous(from_runs(attn_strided)[:, None, :])[:, 0]
    attn_both = jnp.concatenate([attn_local.reshape(tok_rows, head_dim), strided_home], axis=1)
    wo_both = jnp.concatenate([wo_local, wo_strided], axis=0)
    w_cols = wo_both
    mixed_cols, grad_rows = scatter_head(
        lax.dot_general(
            w_cols,
            attn_both,
            (((0,), (1,)), ((), ())),
            precision=HIGHEST,
            preferred_element_type=jnp.float32,
        ),
        gather_head(grad_out),
    )
    mixed = mixed_cols.T
    w_cols = wo_both
    grad_both = lax.dot_general(
        grad_rows.astype(jnp.float32),
        w_cols,
        (((1,), (1,)), ((), ())),
        precision=HIGHEST,
        preferred_element_type=jnp.float32,
    )
    grad_local = grad_both[:, :head_dim]
    grad_strided = to_strided(grad_both[:, head_dim:][:, None, :])[:, 0]
    dq_local, dk_local, dv_local = attend_backward(
        local_q, local_k, local_v, probs_local, attn_local, grad_local.reshape(local_layout)
    )
    dq_strided, dk_strided, dv_strided = attend_backward(
        strided_q, strided_k, strided_v, probs_strided, attn_strided, to_runs(grad_strided)
    )
    strided_grads = jnp.stack(
        [from_runs(dq_strided), from_runs(dk_strided), from_runs(dv_strided)], axis=1
    )
    grads_home = to_contiguous(strided_grads)
    grad_queries = dq_local.reshape(tok_rows, head_dim) + grads_home[:, 0]
    grad_keys = dk_local.reshape(tok_rows, head_dim) + grads_home[:, 1]
    grad_values = dv_local.reshape(tok_rows, head_dim) + grads_home[:, 2]
    return (mixed, grad_queries, grad_keys, grad_values)


def solution(mesh):
    seq_size, head_size = mesh.devices.shape
    zh = 2
    xs = 4
    view = jax.sharding.Mesh(mesh.devices.reshape(seq_size, zh, xs, head_size // (zh * xs)), ("seq",) + HEAD_AXES)
    return jax.shard_map(
        local,
        mesh=view,
        in_specs=(
            P("seq", HEAD_AXES),
            P("seq", HEAD_AXES),
            P("seq", HEAD_AXES),
            P(),
            P(HEAD_AXES, None),
            P(HEAD_AXES, None),
            P("seq", HEAD_AXES),
        ),
        out_specs=(P("seq", HEAD_AXES), P("seq", HEAD_AXES), P("seq", HEAD_AXES), P("seq", HEAD_AXES)),
        check_vma=False,
    )
```

```python
import jax
import jax.numpy as jnp
from jax import lax
from jax.sharding import PartitionSpec as P

HDIM = 128
BLOCK = 128
GROUP_BLK = 2
STRIDE = 128


HIGHEST = lax.Precision.HIGHEST


HEAD_AXES = ("zh", "x", "y")


def swapped(x, axis, distance):
    return lax.ppermute(x, axis, [(i, i ^ 1 << distance) for i in range(lax.axis_size(axis))])


def pair_sum(partial_value):
    return partial_value + swapped(partial_value, "y", 0)


def head_index():
    return (lax.axis_index("zh") * lax.axis_size("x") + lax.axis_index("x")) * lax.axis_size("y") + lax.axis_index("y")


def scatter_head(partial_value, companion):
    sizes = [lax.axis_size(a) for a in HEAD_AXES]
    rows, cols = partial_value.shape
    block = rows // (sizes[0] * sizes[1] * sizes[2])
    parts = partial_value.reshape(*sizes, block, cols)
    return lax.all_to_all(parts, "x", 1, 1, tiled=True).sum(1), companion


def finish_scatter(parts):
    parts = lax.all_to_all(parts, "y", 1, 1, tiled=True).sum(1)
    own = lax.axis_index("zh")
    kept = lax.dynamic_index_in_dim(parts, own, 0, keepdims=False)
    sent = lax.dynamic_index_in_dim(parts, 1 - own, 0, keepdims=False)
    return kept + swapped(sent, "zh", 0)


def gather_head(piece):
    rows, cols = piece.shape
    other = swapped(piece, "zh", 0)
    first = lax.axis_index("zh") == 0
    stacked = jnp.stack([jnp.where(first, piece, other), jnp.where(first, other, piece)])
    for axis in ("y", "x"):
        count = lax.axis_size(axis)
        copies = jnp.broadcast_to(stacked[None], (count,) + stacked.shape)
        stacked = lax.all_to_all(copies, axis, 0, 0, tiled=True)
    order = stacked.reshape(stacked.shape[:3] + (rows, cols)).transpose(3, 2, 0, 1, 4)
    return order.reshape(rows, -1)


def attend_forward(query_part, key_part, value_part, allowed):
    scale_factor = HDIM ** (-0.5)
    partial_value = jnp.einsum("bqhd,bkhd->bhqk", query_part, key_part, precision=HIGHEST)
    scores = pair_sum(partial_value) * scale_factor
    row_max = jnp.max(jnp.where(allowed, scores, -jnp.inf), axis=-1, keepdims=True)
    weights = jnp.where(allowed, jnp.exp(scores - row_max), 0.0)
    probs = weights / jnp.sum(weights, axis=-1, keepdims=True)
    attended = jnp.einsum("bhqk,bkhd->bqhd", probs, value_part, precision=HIGHEST)
    return (attended, probs)


def attend_backward(query_part, key_part, value_part, probs, attended, incoming):
    scale_factor = HDIM ** (-0.5)
    dprobs_part = jnp.einsum("bqhd,bkhd->bhqk", incoming, value_part, precision=HIGHEST)
    delta_part = jnp.transpose(jnp.sum(incoming * attended, axis=-1), (0, 2, 1))[..., None]
    joined = pair_sum(jnp.concatenate([dprobs_part, delta_part], axis=-1))
    dprobs = joined[..., :-1]
    row_delta = joined[..., -1:]
    dscores = probs * (dprobs - row_delta)
    grad_query = jnp.einsum("bhqk,bkhd->bqhd", dscores, key_part, precision=HIGHEST) * scale_factor
    grad_key = jnp.einsum("bhqk,bqhd->bkhd", dscores, query_part, precision=HIGHEST) * scale_factor
    grad_value = jnp.einsum("bhqk,bqhd->bkhd", probs, incoming, precision=HIGHEST)
    return (grad_query, grad_key, grad_value)


def to_strided(stacked):
    seq_devices = lax.axis_size("seq")
    tok_rows, members, head_dim = stacked.shape
    layout = stacked.reshape(tok_rows // seq_devices, seq_devices, members, head_dim)
    moved = lax.all_to_all(layout, "seq", split_axis=1, concat_axis=0, tiled=True)
    return moved.reshape(tok_rows, members, head_dim)


def to_contiguous(stacked):
    seq_devices = lax.axis_size("seq")
    tok_rows, members, head_dim = stacked.shape
    layout = stacked.reshape(seq_devices, tok_rows // seq_devices, 1, members, head_dim)
    moved = lax.all_to_all(layout, "seq", split_axis=0, concat_axis=2, tiled=True)
    return moved.reshape(tok_rows, members, head_dim)


def local(queries, keys, values, local_span, wo_local, wo_strided, grad_out):
    tok_rows, head_dim = queries.shape
    seq_devices = lax.axis_size("seq")
    per_run = STRIDE // seq_devices
    runs_here = tok_rows // per_run
    group_len = GROUP_BLK * BLOCK
    local_layout = (tok_rows // group_len, group_len, 1, head_dim)
    own_span = local_span[head_index() // 2]
    stacked = jnp.stack([queries, keys, values], axis=1)
    spread = to_strided(stacked)
    local_q = queries.reshape(local_layout)
    local_k = keys.reshape(local_layout)
    local_v = values.reshape(local_layout)
    position = jnp.arange(group_len)
    block_of = position // BLOCK
    causal = position[None, :] <= position[:, None]
    reach = block_of[:, None] - block_of[None, :] < own_span
    allowed_local = (causal & reach)[None, None]
    attn_local, probs_local = attend_forward(local_q, local_k, local_v, allowed_local)

    def to_runs(matrix):
        return matrix.reshape(runs_here, per_run, 1, head_dim).transpose(1, 0, 2, 3)

    def from_runs(arranged):
        return arranged.transpose(1, 0, 2, 3).reshape(tok_rows, head_dim)

    strided_q = to_runs(spread[:, 0])
    strided_k = to_runs(spread[:, 1])
    strided_v = to_runs(spread[:, 2])
    order = jnp.arange(runs_here)
    allowed_strided = (order[None, :] <= order[:, None])[None, None]
    attn_strided, probs_strided = attend_forward(strided_q, strided_k, strided_v, allowed_strided)
    strided_home = to_contiguous(from_runs(attn_strided)[:, None, :])[:, 0]
    attn_both = jnp.concatenate([attn_local.reshape(tok_rows, head_dim), strided_home], axis=1)
    wo_both = jnp.concatenate([wo_local, wo_strided], axis=0)
    w_cols = wo_both
    mixed_cols, grad_rows = scatter_head(
        lax.dot_general(
            w_cols,
            attn_both,
            (((0,), (1,)), ((), ())),
            precision=HIGHEST,
            preferred_element_type=jnp.float32,
        ),
        gather_head(grad_out),
    )
    mixed_stage = mixed_cols
    w_cols = wo_both
    grad_both = lax.dot_general(
        grad_rows.astype(jnp.float32),
        w_cols,
        (((1,), (1,)), ((), ())),
        precision=HIGHEST,
        preferred_element_type=jnp.float32,
    )
    grad_local = grad_both[:, :head_dim]
    grad_strided = to_strided(grad_both[:, head_dim:][:, None, :])[:, 0]
    dq_local, dk_local, dv_local = attend_backward(
        local_q, local_k, local_v, probs_local, attn_local, grad_local.reshape(local_layout)
    )
    mixed_stage, dq_local = lax.optimization_barrier((mixed_stage, dq_local))
    mixed = finish_scatter(mixed_stage).T
    dq_strided, dk_strided, dv_strided = attend_backward(
        strided_q, strided_k, strided_v, probs_strided, attn_strided, to_runs(grad_strided)
    )
    strided_grads = jnp.stack(
        [from_runs(dq_strided), from_runs(dk_strided), from_runs(dv_strided)], axis=1
    )
    grads_home = to_contiguous(strided_grads)
    grad_queries = dq_local.reshape(tok_rows, head_dim) + grads_home[:, 0]
    grad_keys = dk_local.reshape(tok_rows, head_dim) + grads_home[:, 1]
    grad_values = dv_local.reshape(tok_rows, head_dim) + grads_home[:, 2]
    return (mixed, grad_queries, grad_keys, grad_values)


def solution(mesh):
    seq_size, head_size = mesh.devices.shape
    zh = 2
    xs = 4
    view = jax.sharding.Mesh(mesh.devices.reshape(seq_size, zh, xs, head_size // (zh * xs)), ("seq",) + HEAD_AXES)
    return jax.shard_map(
        local,
        mesh=view,
        in_specs=(
            P("seq", HEAD_AXES),
            P("seq", HEAD_AXES),
            P("seq", HEAD_AXES),
            P(),
            P(HEAD_AXES, None),
            P(HEAD_AXES, None),
            P("seq", HEAD_AXES),
        ),
        out_specs=(P("seq", HEAD_AXES), P("seq", HEAD_AXES), P("seq", HEAD_AXES), P("seq", HEAD_AXES)),
        check_vma=False,
    )
```

```python
import jax
import jax.numpy as jnp
from jax import lax
from jax.sharding import PartitionSpec as P

HDIM = 128
BLOCK = 128
GROUP_BLK = 2
STRIDE = 128


HIGHEST = lax.Precision.HIGHEST


HEAD_AXES = ("zh", "x", "y")


def swapped(x, axis, distance):
    return lax.ppermute(x, axis, [(i, i ^ 1 << distance) for i in range(lax.axis_size(axis))])


def pair_sum(partial_value):
    return partial_value + swapped(partial_value, "y", 0)


def head_index():
    return (lax.axis_index("zh") * lax.axis_size("x") + lax.axis_index("x")) * lax.axis_size("y") + lax.axis_index("y")


def scatter_head(partial_value, companion):
    sizes = [lax.axis_size(a) for a in HEAD_AXES]
    rows, cols = partial_value.shape
    block = rows // (sizes[0] * sizes[1] * sizes[2])
    parts = partial_value.reshape(*sizes, block, cols)
    return lax.all_to_all(parts, "x", 1, 1, tiled=True).sum(1), companion


def finish_scatter(parts):
    parts = lax.all_to_all(parts, "y", 1, 1, tiled=True).sum(1)
    own = lax.axis_index("zh")
    kept = lax.dynamic_index_in_dim(parts, own, 0, keepdims=False)
    sent = lax.dynamic_index_in_dim(parts, 1 - own, 0, keepdims=False)
    return kept + swapped(sent, "zh", 0)


def gather_head(piece):
    rows, cols = piece.shape
    other = swapped(piece, "zh", 0)
    first = lax.axis_index("zh") == 0
    stacked = jnp.stack([jnp.where(first, piece, other), jnp.where(first, other, piece)])
    for axis in ("y", "x"):
        count = lax.axis_size(axis)
        copies = jnp.broadcast_to(stacked[None], (count,) + stacked.shape)
        stacked = lax.all_to_all(copies, axis, 0, 0, tiled=True)
    order = stacked.reshape(stacked.shape[:3] + (rows, cols)).transpose(3, 2, 0, 1, 4)
    return order.reshape(rows, -1)


def attend_forward(query_part, key_part, value_part, allowed):
    scale_factor = HDIM ** (-0.5)
    partial_value = jnp.einsum("bqhd,bkhd->bhqk", query_part, key_part, precision=HIGHEST)
    scores = pair_sum(partial_value) * scale_factor
    row_max = jnp.max(jnp.where(allowed, scores, -jnp.inf), axis=-1, keepdims=True)
    weights = jnp.where(allowed, jnp.exp(scores - row_max), 0.0)
    probs = weights / jnp.sum(weights, axis=-1, keepdims=True)
    attended = jnp.einsum("bhqk,bkhd->bqhd", probs, value_part, precision=HIGHEST)
    return (attended, probs)


def attend_backward(query_part, key_part, value_part, probs, attended, incoming):
    scale_factor = HDIM ** (-0.5)
    dprobs_part = jnp.einsum("bqhd,bkhd->bhqk", incoming, value_part, precision=HIGHEST)
    delta_part = jnp.transpose(jnp.sum(incoming * attended, axis=-1), (0, 2, 1))[..., None]
    joined = pair_sum(jnp.concatenate([dprobs_part, delta_part], axis=-1))
    dprobs = joined[..., :-1]
    row_delta = joined[..., -1:]
    dscores = probs * (dprobs - row_delta)
    grad_query = jnp.einsum("bhqk,bkhd->bqhd", dscores, key_part, precision=HIGHEST) * scale_factor
    grad_key = jnp.einsum("bhqk,bqhd->bkhd", dscores, query_part, precision=HIGHEST) * scale_factor
    grad_value = jnp.einsum("bhqk,bqhd->bkhd", probs, incoming, precision=HIGHEST)
    return (grad_query, grad_key, grad_value)


def to_strided(stacked):
    seq_devices = lax.axis_size("seq")
    tok_rows, members, head_dim = stacked.shape
    layout = stacked.reshape(tok_rows // seq_devices, seq_devices, members, head_dim)
    moved = lax.all_to_all(layout, "seq", split_axis=1, concat_axis=0, tiled=True)
    return moved.reshape(tok_rows, members, head_dim)


def to_contiguous(stacked):
    seq_devices = lax.axis_size("seq")
    tok_rows, members, head_dim = stacked.shape
    layout = stacked.reshape(seq_devices, tok_rows // seq_devices, 1, members, head_dim)
    moved = lax.all_to_all(layout, "seq", split_axis=0, concat_axis=2, tiled=True)
    return moved.reshape(tok_rows, members, head_dim)


def local(queries, keys, values, local_span, wo_local, wo_strided, grad_out):
    tok_rows, head_dim = queries.shape
    seq_devices = lax.axis_size("seq")
    per_run = STRIDE // seq_devices
    runs_here = tok_rows // per_run
    group_len = GROUP_BLK * BLOCK
    local_layout = (tok_rows // group_len, group_len, 1, head_dim)
    own_span = local_span[head_index() // 2]
    stacked = jnp.stack([queries, keys, values], axis=1)
    spread = to_strided(stacked)
    local_q = queries.reshape(local_layout)
    local_k = keys.reshape(local_layout)
    local_v = values.reshape(local_layout)
    position = jnp.arange(group_len)
    block_of = position // BLOCK
    causal = position[None, :] <= position[:, None]
    reach = block_of[:, None] - block_of[None, :] < own_span
    allowed_local = (causal & reach)[None, None]
    attn_local, probs_local = attend_forward(local_q, local_k, local_v, allowed_local)

    def to_runs(matrix):
        return matrix.reshape(runs_here, per_run, 1, head_dim).transpose(1, 0, 2, 3)

    def from_runs(arranged):
        return arranged.transpose(1, 0, 2, 3).reshape(tok_rows, head_dim)

    strided_q = to_runs(spread[:, 0])
    strided_k = to_runs(spread[:, 1])
    strided_v = to_runs(spread[:, 2])
    order = jnp.arange(runs_here)
    allowed_strided = (order[None, :] <= order[:, None])[None, None]
    attn_strided, probs_strided = attend_forward(strided_q, strided_k, strided_v, allowed_strided)
    strided_home = to_contiguous(from_runs(attn_strided)[:, None, :])[:, 0]
    attn_both = jnp.concatenate([attn_local.reshape(tok_rows, head_dim), strided_home], axis=1)
    wo_both = jnp.concatenate([wo_local, wo_strided], axis=0)
    w_cols = wo_both
    mixed_cols, grad_rows = scatter_head(
        lax.dot_general(
            w_cols,
            attn_both,
            (((0,), (1,)), ((), ())),
            precision=HIGHEST,
            preferred_element_type=jnp.float32,
        ),
        gather_head(grad_out),
    )
    mixed_stage = mixed_cols
    w_cols = wo_both
    grad_both = lax.dot_general(
        grad_rows.astype(jnp.float32),
        w_cols,
        (((1,), (1,)), ((), ())),
        precision=HIGHEST,
        preferred_element_type=jnp.float32,
    )
    grad_local = grad_both[:, :head_dim]
    grad_strided = to_strided(grad_both[:, head_dim:][:, None, :])[:, 0]
    dq_local, dk_local, dv_local = attend_backward(
        local_q, local_k, local_v, probs_local, attn_local, grad_local.reshape(local_layout)
    )
    mixed_stage, dq_local = lax.optimization_barrier((mixed_stage, dq_local))
    mixed = finish_scatter(mixed_stage).T
    dq_strided, dk_strided, dv_strided = attend_backward(
        strided_q, strided_k, strided_v, probs_strided, attn_strided, to_runs(grad_strided)
    )
    strided_grads = jnp.stack(
        [from_runs(dq_strided), from_runs(dk_strided), from_runs(dv_strided)], axis=1
    )
    strided_grads, dq_local = lax.optimization_barrier((strided_grads, dq_local))
    grads_home = to_contiguous(strided_grads)
    grad_queries = dq_local.reshape(tok_rows, head_dim) + grads_home[:, 0]
    grad_keys = dk_local.reshape(tok_rows, head_dim) + grads_home[:, 1]
    grad_values = dv_local.reshape(tok_rows, head_dim) + grads_home[:, 2]
    return (mixed, grad_queries, grad_keys, grad_values)


def solution(mesh):
    seq_size, head_size = mesh.devices.shape
    zh = 2
    xs = 4
    view = jax.sharding.Mesh(mesh.devices.reshape(seq_size, zh, xs, head_size // (zh * xs)), ("seq",) + HEAD_AXES)
    return jax.shard_map(
        local,
        mesh=view,
        in_specs=(
            P("seq", HEAD_AXES),
            P("seq", HEAD_AXES),
            P("seq", HEAD_AXES),
            P(),
            P(HEAD_AXES, None),
            P(HEAD_AXES, None),
            P("seq", HEAD_AXES),
        ),
        out_specs=(P("seq", HEAD_AXES), P("seq", HEAD_AXES), P("seq", HEAD_AXES), P("seq", HEAD_AXES)),
        check_vma=False,
    )
```

```python
import jax
import jax.numpy as jnp
from jax import lax
from jax.sharding import PartitionSpec as P

HDIM = 128
BLOCK = 128
GROUP_BLK = 2
STRIDE = 128


HIGHEST = lax.Precision.HIGHEST


HEAD_AXES = ("zh", "x", "y")


def swapped(x, axis, distance):
    return lax.ppermute(x, axis, [(i, i ^ 1 << distance) for i in range(lax.axis_size(axis))])


def pair_sum(partial_value):
    return partial_value + swapped(partial_value, "y", 0)


def head_index():
    return (lax.axis_index("zh") * lax.axis_size("x") + lax.axis_index("x")) * lax.axis_size("y") + lax.axis_index("y")


def scatter_head(partial_value, companion):
    sizes = [lax.axis_size(a) for a in HEAD_AXES]
    rows, cols = partial_value.shape
    block = rows // (sizes[0] * sizes[1] * sizes[2])
    parts = partial_value.reshape(*sizes, block, cols)
    return lax.all_to_all(parts, "x", 1, 1, tiled=True).sum(1), companion


def finish_scatter(parts):
    parts = lax.all_to_all(parts, "y", 1, 1, tiled=True).sum(1)
    own = lax.axis_index("zh")
    return lax.dynamic_index_in_dim(parts + swapped(parts, "zh", 0), own, 0, keepdims=False)


def gather_head(piece):
    rows, cols = piece.shape
    other = swapped(piece, "zh", 0)
    first = lax.axis_index("zh") == 0
    stacked = jnp.stack([jnp.where(first, piece, other), jnp.where(first, other, piece)])
    for axis in ("y", "x"):
        count = lax.axis_size(axis)
        copies = jnp.broadcast_to(stacked[None], (count,) + stacked.shape)
        stacked = lax.all_to_all(copies, axis, 0, 0, tiled=True)
    order = stacked.reshape(stacked.shape[:3] + (rows, cols)).transpose(3, 2, 0, 1, 4)
    return order.reshape(rows, -1)


def attend_forward(query_part, key_part, value_part, allowed):
    scale_factor = HDIM ** (-0.5)
    partial_value = jnp.einsum("bqhd,bkhd->bhqk", query_part, key_part, precision=HIGHEST)
    scores = pair_sum(partial_value) * scale_factor
    row_max = jnp.max(jnp.where(allowed, scores, -jnp.inf), axis=-1, keepdims=True)
    weights = jnp.where(allowed, jnp.exp(scores - row_max), 0.0)
    probs = weights / jnp.sum(weights, axis=-1, keepdims=True)
    attended = jnp.einsum("bhqk,bkhd->bqhd", probs, value_part, precision=HIGHEST)
    return (attended, probs)


def attend_backward(query_part, key_part, value_part, probs, attended, incoming):
    scale_factor = HDIM ** (-0.5)
    dprobs_part = jnp.einsum("bqhd,bkhd->bhqk", incoming, value_part, precision=HIGHEST)
    delta_part = jnp.transpose(jnp.sum(incoming * attended, axis=-1), (0, 2, 1))[..., None]
    joined = pair_sum(jnp.concatenate([dprobs_part, delta_part], axis=-1))
    dprobs = joined[..., :-1]
    row_delta = joined[..., -1:]
    dscores = probs * (dprobs - row_delta)
    grad_query = jnp.einsum("bhqk,bkhd->bqhd", dscores, key_part, precision=HIGHEST) * scale_factor
    grad_key = jnp.einsum("bhqk,bqhd->bkhd", dscores, query_part, precision=HIGHEST) * scale_factor
    grad_value = jnp.einsum("bhqk,bqhd->bkhd", probs, incoming, precision=HIGHEST)
    return (grad_query, grad_key, grad_value)


def to_strided(stacked):
    seq_devices = lax.axis_size("seq")
    tok_rows, members, head_dim = stacked.shape
    layout = stacked.reshape(tok_rows // seq_devices, seq_devices, members, head_dim)
    moved = lax.all_to_all(layout, "seq", split_axis=1, concat_axis=0, tiled=True)
    return moved.reshape(tok_rows, members, head_dim)


def to_contiguous(stacked):
    seq_devices = lax.axis_size("seq")
    tok_rows, members, head_dim = stacked.shape
    layout = stacked.reshape(seq_devices, tok_rows // seq_devices, 1, members, head_dim)
    moved = lax.all_to_all(layout, "seq", split_axis=0, concat_axis=2, tiled=True)
    return moved.reshape(tok_rows, members, head_dim)


def local(queries, keys, values, local_span, wo_local, wo_strided, grad_out):
    tok_rows, head_dim = queries.shape
    seq_devices = lax.axis_size("seq")
    per_run = STRIDE // seq_devices
    runs_here = tok_rows // per_run
    group_len = GROUP_BLK * BLOCK
    local_layout = (tok_rows // group_len, group_len, 1, head_dim)
    own_span = local_span[head_index() // 2]
    stacked = jnp.stack([queries, keys, values], axis=1)
    spread = to_strided(stacked)
    local_q = queries.reshape(local_layout)
    local_k = keys.reshape(local_layout)
    local_v = values.reshape(local_layout)
    position = jnp.arange(group_len)
    block_of = position // BLOCK
    causal = position[None, :] <= position[:, None]
    reach = block_of[:, None] - block_of[None, :] < own_span
    allowed_local = (causal & reach)[None, None]
    attn_local, probs_local = attend_forward(local_q, local_k, local_v, allowed_local)

    def to_runs(matrix):
        return matrix.reshape(runs_here, per_run, 1, head_dim).transpose(1, 0, 2, 3)

    def from_runs(arranged):
        return arranged.transpose(1, 0, 2, 3).reshape(tok_rows, head_dim)

    strided_q = to_runs(spread[:, 0])
    strided_k = to_runs(spread[:, 1])
    strided_v = to_runs(spread[:, 2])
    order = jnp.arange(runs_here)
    allowed_strided = (order[None, :] <= order[:, None])[None, None]
    attn_strided, probs_strided = attend_forward(strided_q, strided_k, strided_v, allowed_strided)
    strided_home = to_contiguous(from_runs(attn_strided)[:, None, :])[:, 0]
    attn_both = jnp.concatenate([attn_local.reshape(tok_rows, head_dim), strided_home], axis=1)
    wo_both = jnp.concatenate([wo_local, wo_strided], axis=0)
    w_cols = wo_both
    mixed_cols, grad_rows = scatter_head(
        lax.dot_general(
            w_cols,
            attn_both,
            (((0,), (1,)), ((), ())),
            precision=HIGHEST,
            preferred_element_type=jnp.float32,
        ),
        gather_head(grad_out),
    )
    mixed_stage = mixed_cols
    w_cols = wo_both
    grad_both = lax.dot_general(
        grad_rows.astype(jnp.float32),
        w_cols,
        (((1,), (1,)), ((), ())),
        precision=HIGHEST,
        preferred_element_type=jnp.float32,
    )
    grad_local = grad_both[:, :head_dim]
    grad_strided = to_strided(grad_both[:, head_dim:][:, None, :])[:, 0]
    dq_local, dk_local, dv_local = attend_backward(
        local_q, local_k, local_v, probs_local, attn_local, grad_local.reshape(local_layout)
    )
    mixed_stage, dq_local = lax.optimization_barrier((mixed_stage, dq_local))
    mixed = finish_scatter(mixed_stage).T
    dq_strided, dk_strided, dv_strided = attend_backward(
        strided_q, strided_k, strided_v, probs_strided, attn_strided, to_runs(grad_strided)
    )
    strided_grads = jnp.stack(
        [from_runs(dq_strided), from_runs(dk_strided), from_runs(dv_strided)], axis=1
    )
    grads_home = to_contiguous(strided_grads)
    grad_queries = dq_local.reshape(tok_rows, head_dim) + grads_home[:, 0]
    grad_keys = dk_local.reshape(tok_rows, head_dim) + grads_home[:, 1]
    grad_values = dv_local.reshape(tok_rows, head_dim) + grads_home[:, 2]
    return (mixed, grad_queries, grad_keys, grad_values)


def solution(mesh):
    seq_size, head_size = mesh.devices.shape
    zh = 2
    xs = 4
    view = jax.sharding.Mesh(mesh.devices.reshape(seq_size, zh, xs, head_size // (zh * xs)), ("seq",) + HEAD_AXES)
    return jax.shard_map(
        local,
        mesh=view,
        in_specs=(
            P("seq", HEAD_AXES),
            P("seq", HEAD_AXES),
            P("seq", HEAD_AXES),
            P(),
            P(HEAD_AXES, None),
            P(HEAD_AXES, None),
            P("seq", HEAD_AXES),
        ),
        out_specs=(P("seq", HEAD_AXES), P("seq", HEAD_AXES), P("seq", HEAD_AXES), P("seq", HEAD_AXES)),
        check_vma=False,
    )
```
